256 devices in a mesh: pipe: 4 (over z_hi), dp: 64 (over y, x, z_lo, core).
Axes of the slice: x: 4, y: 4, z: 8 (z_hi: 4, z_lo: 2; z = z_hi * 2 + z_lo), core: 2. Of those that a mesh axis runs over, the one named last changes fastest.
Arguments:
- acts_in: bfloat16 [2, 4096, 4096], P(None, 'dp'), may hold values from -40 to 40
- cotangent: bfloat16 [2, 4096, 4096], P(None, 'dp'), may hold values from -6 to 6
- norm_gains: float32 [4, 4096], P('pipe'), may hold values from 0.1 to 1.9
- weights: bfloat16 [4, 256, 128, 128], P('pipe', 'dp'), may hold values from -0.1875 to 0.1875
- tile_columns: int32 [4, 256], P('pipe'), may hold values from 0 to 31, as said below
- lengths: int32 [2, 64], P(None, 'dp'), may hold values from 16 to 64
Outputs:
- section_out: bfloat16 [4, 2, 4096, 4096], P('pipe', None, 'dp')
- input_grad: bfloat16 [4, 2, 4096, 4096], P('pipe', None, 'dp')
- weight_grad: float32 [4, 256, 128, 128], P('pipe', 'dp')
The draws below stay inside these ranges and needn't reach their ends.
Inputs may be any that keep to these rules, and one draw needn't show every extreme that they name: `tile_columns`: the 8 entries of one block row of a section (positions r * 8 to r * 8 + 7) are distinct.
All inputs are finite; a program needn't handle non-finite values.
Results may differ from the reference program's by a relative error of at most 0.0081.
Values may be sent and summed in bfloat16 or wider, within the bound.
No kernel may reach another device: no remote copies, remote signals or barrier semaphores. Data moves between devices by JAX's collectives and lax.ppermute only.
A program may use at most 384 MiB of HBM per device.

```python
import math
import jax
import jax.numpy as jnp
from jax import lax

D = 4096
TILE = 128
KEEP = 8
M = 2
BLOCKS = 32
TILES = 256
TOKENS = 4096
LENGTH = 64
SEQS = 64
N_PIPE = 4


def draw_acts_in(key, part):
    shape_all = (M, TOKENS, D)
    keys = jax.random.split(key, 3)
    base = jax.random.truncated_normal(keys[0], -6.0, 6.0, shape_all, jnp.float32)
    row_scale = jnp.exp(jax.random.uniform(keys[1], (M, TOKENS, 1), jnp.float32, math.log(0.3), math.log(3.0)))
    column_scale = jnp.exp(jax.random.uniform(keys[2], (1, 1, D), jnp.float32, math.log(0.3), math.log(3.0)))
    return jnp.clip(base * row_scale * column_scale, -40.0, 40.0).astype(jnp.bfloat16)


def draw_tile_columns(key, part):
    row_keys = jax.random.split(jax.random.fold_in(key, 11), N_PIPE * BLOCKS)
    orders = jax.vmap(lambda row_key: jax.random.permutation(row_key, BLOCKS))(row_keys)
    return orders[:, :KEEP].reshape(N_PIPE, BLOCKS * KEEP).astype(jnp.int32)


def plant(result, own_key, least, high):
    longest = result.shape.index(max(result.shape))
    spots = []
    for shift in (0, 1):
        where = [jax.random.randint(jax.random.fold_in(own_key, axis), (), 0, length) for axis, length in enumerate(result.shape)]
        where[longest] = (where[longest] + shift) % result.shape[longest]
        spots.append(tuple(where))
    return result.at[spots[0]].set(least).at[spots[1]].set(high)


def block_scale(key, extent, shards, low, top_value):
    factor_of, own = 1.0, jax.random.fold_in(key, 6)
    for axis_at, parts in shards:
        steps = jnp.exp(jax.random.uniform(jax.random.fold_in(own, axis_at), (parts,), jnp.float32, low / len(shards), top_value / len(shards)))
        factor_of = factor_of * jnp.repeat(steps, extent[axis_at] // parts).reshape([-1 if axis == axis_at else 1 for axis in range(len(extent))])
    return factor_of


def normal_values(key, shape, deviation, limit, shards=(), held_as=jnp.bfloat16):
    array = deviation * jax.random.normal(key, shape, jnp.float32)
    if shards:
        array = array * block_scale(key, shape, shards, -0.22, 0.18)
    return jnp.clip(array, -limit, limit).astype(held_as)


def setup_inputs(seed: int = 0) -> dict:
    key_of = jax.random.split(jax.random.key(seed), 7)
    acts_in = draw_acts_in(jax.random.fold_in(key_of[6], 71), 0)
    cotangent = normal_values(key_of[1], (M, TOKENS, D), 1.0, 6.0, ((1, 64),))
    norm_gains = jnp.clip(1.0 + 0.18 * jax.random.normal(key_of[2], (N_PIPE, D), jnp.float32), 0.1, 1.9)
    weights = normal_values(key_of[3], (N_PIPE, TILES, TILE, TILE), (KEEP * TILE) ** -0.5, 0.1875, ((0, 4), (1, 64)))
    tile_columns = draw_tile_columns(jax.random.fold_in(key_of[6], 71), 0)
    lengths = plant(jax.random.randint(key_of[5], (M, SEQS), LENGTH // 4, LENGTH + 1), jax.random.fold_in(key_of[5], 1), LENGTH // 4, LENGTH).astype(jnp.int32)
    return {"acts_in": acts_in, "cotangent": cotangent, "norm_gains": norm_gains, "weights": weights, "tile_columns": tile_columns, "lengths": lengths}


epsilon = 1e-05

def row_mask(length_row):
    position = jnp.arange(TOKENS, dtype=jnp.int32)
    sequence = position // LENGTH
    within = position - sequence * LENGTH
    match_table = sequence[:, None] == jnp.arange(SEQS, dtype=jnp.int32)[None, :]
    length_limit = lax.optimization_barrier(jnp.sum(jnp.where(match_table, length_row[None, :], 0), axis=1))
    return (within < length_limit).astype(jnp.float32)

def normalize(section_input, section_gain):
    values = section_input.astype(jnp.float32)
    inv_rms = lax.rsqrt(lax.optimization_barrier(jnp.mean(values * values, axis=-1, keepdims=True)) + epsilon)
    unit_rows = values * inv_rms
    return (values, inv_rms, unit_rows, (unit_rows * section_gain).astype(jnp.bfloat16))

def block_rows_of(hidden):
    return jnp.transpose(hidden.astype(jnp.float32).reshape(TOKENS, BLOCKS, TILE), (1, 0, 2))

def sparse_forward(hidden, tile_grid, column_table):

    def add_block(total_sum, pieces):
        block_rows, block_tiles, block_columns = pieces
        contrib = jnp.einsum('tk,jkn->tjn', block_rows, block_tiles.astype(jnp.float32), precision=lax.Precision.HIGHEST)
        return (total_sum.at[:, block_columns, :].add(contrib), None)
    start_sum = jnp.zeros((TOKENS, BLOCKS, TILE), jnp.float32)
    total_sum, unused = lax.scan(add_block, start_sum, (block_rows_of(hidden), tile_grid, column_table))
    return total_sum.reshape(TOKENS, D)

def sparse_backward(hidden, pre_delta, tile_grid, column_table):
    delta_blocks = pre_delta.astype(jnp.float32).reshape(TOKENS, BLOCKS, TILE)

    def one_block(carried, pieces):
        block_rows, block_tiles, block_columns = pieces
        picked = jnp.take(delta_blocks, block_columns, axis=1)
        tile_grad = jnp.einsum('tk,tjn->jkn', block_rows, picked, precision=lax.Precision.HIGHEST)
        row_delta = jnp.einsum('tjn,jkn->tk', picked, block_tiles.astype(jnp.float32), precision=lax.Precision.HIGHEST)
        return (carried, (tile_grad, row_delta))
    carried, outcome = lax.scan(one_block, jnp.zeros((), jnp.float32), (block_rows_of(hidden), tile_grid, column_table))
    tile_grads, row_deltas = outcome
    return (tile_grads.reshape(TILES, TILE, TILE), jnp.transpose(row_deltas, (1, 0, 2)).reshape(TOKENS, D))

def reference(acts_in, cotangent, norm_gains, weights, tile_columns, lengths):
    grids = weights.reshape(N_PIPE, BLOCKS, KEEP, TILE, TILE)
    tables = tile_columns.reshape(N_PIPE, BLOCKS, KEEP).astype(jnp.int32)
    outputs = [[None] * M for section_id in range(N_PIPE)]
    grads = [[None] * M for section_id in range(N_PIPE)]
    saved = [[None] * M for section_id in range(N_PIPE)]
    for micro_id in range(M):
        section_input = acts_in[micro_id]
        for section_id in range(N_PIPE):
            values, inv_rms, unit_rows, hidden = normalize(section_input, norm_gains[section_id])
            pre_act = sparse_forward(hidden, grids[section_id], tables[section_id])
            section_result = (values + jax.nn.silu(pre_act)).astype(jnp.bfloat16)
            saved[section_id][micro_id] = (section_input, pre_act)
            outputs[section_id][micro_id] = section_result
            section_input = section_result
    tile_sums = [jnp.zeros((TILES, TILE, TILE), jnp.float32) for section_id in range(N_PIPE)]
    for micro_id in range(M):
        grad_input = (cotangent[micro_id].astype(jnp.float32) * row_mask(lengths[micro_id])[:, None]).astype(jnp.bfloat16)
        for section_id in reversed(range(N_PIPE)):
            section_input, pre_act = saved[section_id][micro_id]
            values, inv_rms, unit_rows, hidden = normalize(section_input, norm_gains[section_id])
            sigmoid_part = jax.nn.sigmoid(pre_act)
            grad_float = grad_input.astype(jnp.float32)
            pre_delta = (grad_float * sigmoid_part * (1.0 + pre_act * (1.0 - sigmoid_part))).astype(jnp.bfloat16)
            tile_grad, hidden_delta = sparse_backward(hidden, pre_delta, grids[section_id], tables[section_id])
            tile_sums[section_id] = tile_sums[section_id] + tile_grad
            gained = hidden_delta * norm_gains[section_id]
            input_delta = grad_float + inv_rms * (gained - unit_rows * lax.optimization_barrier(jnp.mean(gained * unit_rows, axis=-1, keepdims=True)))
            grad_input = input_delta.astype(jnp.bfloat16)
            grads[section_id][micro_id] = grad_input
    section_out = jnp.stack([jnp.stack(outputs[section_id]) for section_id in range(N_PIPE)])
    input_grad = jnp.stack([jnp.stack(grads[section_id]) for section_id in range(N_PIPE)])
    return (section_out, input_grad, jnp.stack(tile_sums))
```

```python
import jax
import jax.numpy as jnp
from jax import lax
from jax.sharding import Mesh
from jax.sharding import PartitionSpec as P

TILE = 128
KEEP = 8
GROUP = ("dq", "zl", "core")


epsilon = 1e-05


def normalize(section_input, section_gain):
    values = section_input.astype(jnp.float32)
    inv_rms = lax.rsqrt(jnp.mean(values * values, axis=-1, keepdims=True) + epsilon)
    unit_rows = values * inv_rms
    return (values, inv_rms, unit_rows, (unit_rows * section_gain).astype(jnp.bfloat16))


def store_slot(buffer_all, new_value, micro_slot, is_live):
    old_value = lax.dynamic_index_in_dim(buffer_all, micro_slot, 0, keepdims=False)
    chosen = jnp.where(is_live, new_value, old_value)
    return lax.dynamic_update_index_in_dim(buffer_all, chosen, micro_slot, 0)


def reduce_tiles(tile_grads):
    core = lax.axis_index("core")
    chips = lax.axis_size("dq") * lax.axis_size("zl")
    pairs = tile_grads.reshape((chips, 2, -1) + tile_grads.shape[1:])
    send = lax.dynamic_index_in_dim(pairs, 1 - core, 1, keepdims=False)
    keep = lax.dynamic_index_in_dim(pairs, core, 1, keepdims=False)
    halved = keep + lax.ppermute(send, "core", [(0, 1), (1, 0)])
    spread = lax.all_to_all(halved, ("dq", "zl"), 0, 0, tiled=True)
    return spread.sum(axis=0)


def on_device(acts_in, cotangent, norm_gains, weights, tile_columns, lengths):
    micro_count, row_count, model_width = acts_in.shape
    section_count = lax.axis_size("pipe")
    section_here = lax.axis_index("pipe")
    blocks = model_width // TILE
    section_gain = norm_gains[0]
    column_list = tile_columns[0]
    column_table = column_list.reshape(blocks, KEEP)
    gathered = lax.all_gather(weights[0], GROUP, axis=0, tiled=True)
    tile_grid = gathered.reshape(blocks, KEEP, TILE, TILE)
    onehot = (column_table[:, :, None] == jnp.arange(blocks, dtype=jnp.int32)).astype(jnp.bfloat16)
    dense = (
        jnp.einsum("rjkn,rjc->rkcn", tile_grid, onehot, preferred_element_type=jnp.float32)
        .astype(jnp.bfloat16)
        .reshape(model_width, model_width)
    )
    within = jnp.arange(row_count, dtype=jnp.int32)
    valid_rows = (within[None, :] < lengths).astype(jnp.float32)
    received = jnp.zeros((row_count, model_width), jnp.bfloat16)
    section_out = jnp.zeros_like(acts_in)
    saved_inputs = jnp.zeros_like(acts_in)
    saved_hidden = jnp.zeros_like(acts_in)
    saved_pre = jnp.zeros(acts_in.shape, jnp.float32)

    def run_forward(section_input):
        values, inv_rms, unit_rows, hidden = normalize(section_input, section_gain)
        pre_act = jnp.dot(hidden, dense, preferred_element_type=jnp.float32)
        return ((values + jax.nn.silu(pre_act)).astype(jnp.bfloat16), pre_act, hidden)

    def skip_forward(section_input):
        return (
            section_input,
            jnp.zeros((row_count, model_width), jnp.float32),
            jnp.zeros((row_count, model_width), jnp.bfloat16),
        )

    for clock_tick in range(micro_count + section_count - 1):
        micro_index = clock_tick - section_here
        is_live = jnp.logical_and(micro_index >= 0, micro_index < micro_count)
        micro_slot = jnp.clip(micro_index, 0, micro_count - 1)
        first_input = lax.dynamic_index_in_dim(acts_in, micro_slot, 0, keepdims=False)
        section_input = jnp.where(section_here == 0, first_input, received)
        section_result, pre_act, hidden = lax.cond(
            is_live, run_forward, skip_forward, section_input
        )
        section_out = store_slot(section_out, section_result, micro_slot, is_live)
        saved_inputs = store_slot(saved_inputs, section_input, micro_slot, is_live)
        saved_hidden = store_slot(saved_hidden, hidden, micro_slot, is_live)
        saved_pre = store_slot(saved_pre, pre_act, micro_slot, is_live)
        pairs = [
            (source, source + 1)
            for source in range(section_count - 1)
            if 0 <= clock_tick - source < micro_count
        ]
        if pairs:
            received = lax.ppermute(section_result, "pipe", pairs)

    def run_backward(section_input, grad_input, pre_act):
        values, inv_rms, unit_rows, hidden = normalize(section_input, section_gain)
        sigmoid_part = jax.nn.sigmoid(pre_act)
        grad_float = grad_input.astype(jnp.float32)
        pre_delta = (grad_float * sigmoid_part * (1.0 + pre_act * (1.0 - sigmoid_part))).astype(
            jnp.bfloat16
        )
        hidden_delta = lax.dot_general(
            pre_delta, dense, (((1,), (1,)), ((), ())), preferred_element_type=jnp.float32
        )
        gained = hidden_delta * section_gain
        input_delta = grad_float + inv_rms * (
            gained - unit_rows * jnp.mean(gained * unit_rows, axis=-1, keepdims=True)
        )
        return (input_delta.astype(jnp.bfloat16), pre_delta)

    def skip_backward(section_input, grad_input, pre_act):
        return (grad_input, jnp.zeros_like(grad_input))

    received = jnp.zeros((row_count, model_width), jnp.bfloat16)
    input_grad = jnp.zeros_like(acts_in)
    saved_delta = jnp.zeros_like(acts_in)
    for clock_tick in range(micro_count + section_count - 1):
        micro_index = clock_tick - (section_count - 1 - section_here)
        is_live = jnp.logical_and(micro_index >= 0, micro_index < micro_count)
        micro_slot = jnp.clip(micro_index, 0, micro_count - 1)
        last_cot = lax.dynamic_index_in_dim(cotangent, micro_slot, 0, keepdims=False).astype(
            jnp.float32
        )
        last_mask = lax.dynamic_index_in_dim(valid_rows, micro_slot, 0, keepdims=False)
        last_grad = (last_cot * last_mask[:, None]).astype(jnp.bfloat16)
        grad_input = jnp.where(section_here == section_count - 1, last_grad, received)
        section_input = lax.dynamic_index_in_dim(saved_inputs, micro_slot, 0, keepdims=False)
        pre_act = lax.dynamic_index_in_dim(saved_pre, micro_slot, 0, keepdims=False)
        input_delta, pre_delta = lax.cond(
            is_live, run_backward, skip_backward, section_input, grad_input, pre_act
        )
        input_grad = store_slot(input_grad, input_delta, micro_slot, is_live)
        saved_delta = store_slot(saved_delta, pre_delta, micro_slot, is_live)
        pairs = [
            (source, source - 1)
            for source in range(1, section_count)
            if 0 <= clock_tick - (section_count - 1 - source) < micro_count
        ]
        if pairs:
            received = lax.ppermute(input_delta, "pipe", pairs)
    all_rows = micro_count * row_count
    picked = jnp.take(saved_delta.reshape(all_rows, blocks, TILE), column_table, axis=1)
    tile_grads = jnp.einsum(
        "trk,trjn->rjkn",
        saved_hidden.reshape(all_rows, blocks, TILE),
        picked,
        preferred_element_type=jnp.float32,
    )
    weight_grad = reduce_tiles(tile_grads.reshape(blocks * KEEP, TILE, TILE))
    return (section_out[None], input_grad[None], weight_grad[None])


def solution(mesh):
    dp_size = mesh.shape["dp"]
    split = Mesh(
        mesh.devices.reshape(mesh.shape["pipe"], dp_size // 4, 2, 2),
        ("pipe",) + GROUP,
    )
    placed = (
        P(None, GROUP, None),
        P(None, GROUP, None),
        P("pipe", None),
        P("pipe", GROUP, None, None),
        P("pipe", None),
        P(None, GROUP),
    )
    return jax.shard_map(
        on_device,
        mesh=split,
        in_specs=placed,
        out_specs=(
            P("pipe", None, GROUP, None),
            P("pipe", None, GROUP, None),
            P("pipe", GROUP, None, None),
        ),
        check_vma=False,
    )
```

```python
import jax
import jax.numpy as jnp
from jax import lax
from jax.sharding import Mesh
from jax.sharding import PartitionSpec as P

TILE = 128
KEEP = 8
GROUP = ("dq", "zl", "core")


epsilon = 1e-05


def normalize(section_input, section_gain):
    values = section_input.astype(jnp.float32)
    inv_rms = lax.rsqrt(jnp.mean(values * values, axis=-1, keepdims=True) + epsilon)
    unit_rows = values * inv_rms
    return (values, inv_rms, unit_rows, (unit_rows * section_gain).astype(jnp.bfloat16))


def store_slot(buffer_all, new_value, micro_slot, is_live):
    old_value = lax.dynamic_index_in_dim(buffer_all, micro_slot, 0, keepdims=False)
    chosen = jnp.where(is_live, new_value, old_value)
    return lax.dynamic_update_index_in_dim(buffer_all, chosen, micro_slot, 0)


def reduce_tiles(tile_grads):
    core = lax.axis_index("core")
    chips = lax.axis_size("dq") * lax.axis_size("zl")
    pairs = tile_grads.reshape((chips, 2, -1) + tile_grads.shape[1:])
    send = lax.dynamic_index_in_dim(pairs, 1 - core, 1, keepdims=False)
    keep = lax.dynamic_index_in_dim(pairs, core, 1, keepdims=False)
    halved = keep + lax.ppermute(send, "core", [(0, 1), (1, 0)])
    spread = lax.all_to_all(halved, ("dq", "zl"), 0, 0, tiled=True)
    return spread.sum(axis=0)


def gather_tiles(shard):
    core = lax.axis_index("core")
    chips = lax.axis_size("dq") * lax.axis_size("zl")
    sent = jnp.broadcast_to(shard[None], (chips,) + shard.shape)
    mine = lax.all_to_all(sent, ("dq", "zl"), 0, 0, tiled=True)
    other = lax.ppermute(mine, "core", [(0, 1), (1, 0)])
    both = jnp.where(core == 0, jnp.stack([mine, other], 1), jnp.stack([other, mine], 1))
    return both.reshape((-1,) + shard.shape[1:])


def on_device(acts_in, cotangent, norm_gains, weights, tile_columns, lengths):
    micro_count, row_count, model_width = acts_in.shape
    within = jnp.arange(row_count, dtype=jnp.int32)
    valid_rows = (within[None, :] < lengths).astype(jnp.float32)
    merged = (1, micro_count * row_count, model_width)
    section_out, input_grad, weight_grad = run_pipeline(
        acts_in.reshape(merged),
        cotangent.reshape(merged),
        norm_gains,
        weights,
        tile_columns,
        valid_rows.reshape(merged[:2]),
    )
    return (
        section_out.reshape(acts_in.shape)[None],
        input_grad.reshape(acts_in.shape)[None],
        weight_grad[None],
    )


def run_pipeline(acts_in, cotangent, norm_gains, weights, tile_columns, valid_rows):
    micro_count, row_count, model_width = acts_in.shape
    section_count = lax.axis_size("pipe")
    section_here = lax.axis_index("pipe")
    blocks = model_width // TILE
    section_gain = norm_gains[0]
    column_list = tile_columns[0]
    column_table = column_list.reshape(blocks, KEEP)
    gathered = gather_tiles(weights[0])
    tile_grid = gathered.reshape(blocks, KEEP, TILE, TILE)
    onehot = (column_table[:, :, None] == jnp.arange(blocks, dtype=jnp.int32)).astype(jnp.bfloat16)
    dense = (
        jnp.einsum("rjkn,rjc->rkcn", tile_grid, onehot, preferred_element_type=jnp.float32)
        .astype(jnp.bfloat16)
        .reshape(model_width, model_width)
    )
    received = jnp.zeros((row_count, model_width), jnp.bfloat16)
    section_out = jnp.zeros_like(acts_in)
    saved_inputs = jnp.zeros_like(acts_in)
    saved_hidden = jnp.zeros_like(acts_in)
    saved_pre = jnp.zeros(acts_in.shape, jnp.float32)

    def run_forward(section_input):
        values, inv_rms, unit_rows, hidden = normalize(section_input, section_gain)
        pre_act = jnp.dot(hidden, dense, preferred_element_type=jnp.float32)
        return ((values + jax.nn.silu(pre_act)).astype(jnp.bfloat16), pre_act, hidden)

    def skip_forward(section_input):
        return (
            section_input,
            jnp.zeros((row_count, model_width), jnp.float32),
            jnp.zeros((row_count, model_width), jnp.bfloat16),
        )

    for clock_tick in range(micro_count + section_count - 1):
        micro_index = clock_tick - section_here
        is_live = jnp.logical_and(micro_index >= 0, micro_index < micro_count)
        micro_slot = jnp.clip(micro_index, 0, micro_count - 1)
        first_input = lax.dynamic_index_in_dim(acts_in, micro_slot, 0, keepdims=False)
        section_input = jnp.where(section_here == 0, first_input, received)
        section_result, pre_act, hidden = lax.cond(
            is_live, run_forward, skip_forward, section_input
        )
        section_out = store_slot(section_out, section_result, micro_slot, is_live)
        saved_inputs = store_slot(saved_inputs, section_input, micro_slot, is_live)
        saved_hidden = store_slot(saved_hidden, hidden, micro_slot, is_live)
        saved_pre = store_slot(saved_pre, pre_act, micro_slot, is_live)
        pairs = [
            (source, source + 1)
            for source in range(section_count - 1)
            if 0 <= clock_tick - source < micro_count
        ]
        if pairs:
            received = lax.ppermute(section_result, "pipe", pairs)

    def run_backward(section_input, grad_input, pre_act):
        values, inv_rms, unit_rows, hidden = normalize(section_input, section_gain)
        sigmoid_part = jax.nn.sigmoid(pre_act)
        grad_float = grad_input.astype(jnp.float32)
        pre_delta = (grad_float * sigmoid_part * (1.0 + pre_act * (1.0 - sigmoid_part))).astype(
            jnp.bfloat16
        )
        hidden_delta = lax.dot_general(
            pre_delta, dense, (((1,), (1,)), ((), ())), preferred_element_type=jnp.float32
        )
        gained = hidden_delta * section_gain
        input_delta = grad_float + inv_rms * (
            gained - unit_rows * jnp.mean(gained * unit_rows, axis=-1, keepdims=True)
        )
        return (input_delta.astype(jnp.bfloat16), pre_delta)

    def skip_backward(section_input, grad_input, pre_act):
        return (grad_input, jnp.zeros_like(grad_input))

    received = jnp.zeros((row_count, model_width), jnp.bfloat16)
    input_grad = jnp.zeros_like(acts_in)
    saved_delta = jnp.zeros_like(acts_in)
    for clock_tick in range(micro_count + section_count - 1):
        micro_index = clock_tick - (section_count - 1 - section_here)
        is_live = jnp.logical_and(micro_index >= 0, micro_index < micro_count)
        micro_slot = jnp.clip(micro_index, 0, micro_count - 1)
        last_cot = lax.dynamic_index_in_dim(cotangent, micro_slot, 0, keepdims=False).astype(
            jnp.float32
        )
        last_mask = lax.dynamic_index_in_dim(valid_rows, micro_slot, 0, keepdims=False)
        last_grad = (last_cot * last_mask[:, None]).astype(jnp.bfloat16)
        grad_input = jnp.where(section_here == section_count - 1, last_grad, received)
        section_input = lax.dynamic_index_in_dim(saved_inputs, micro_slot, 0, keepdims=False)
        pre_act = lax.dynamic_index_in_dim(saved_pre, micro_slot, 0, keepdims=False)
        input_delta, pre_delta = lax.cond(
            is_live, run_backward, skip_backward, section_input, grad_input, pre_act
        )
        input_grad = store_slot(input_grad, input_delta, micro_slot, is_live)
        saved_delta = store_slot(saved_delta, pre_delta, micro_slot, is_live)
        pairs = [
            (source, source - 1)
            for source in range(1, section_count)
            if 0 <= clock_tick - (section_count - 1 - source) < micro_count
        ]
        if pairs:
            received = lax.ppermute(input_delta, "pipe", pairs)
    all_rows = micro_count * row_count
    picked = jnp.take(saved_delta.reshape(all_rows, blocks, TILE), column_table, axis=1)
    tile_grads = jnp.einsum(
        "trk,trjn->rjkn",
        saved_hidden.reshape(all_rows, blocks, TILE),
        picked,
        preferred_element_type=jnp.float32,
    )
    weight_grad = reduce_tiles(tile_grads.reshape(blocks * KEEP, TILE, TILE))
    return (section_out, input_grad, weight_grad)


def solution(mesh):
    dp_size = mesh.shape["dp"]
    split = Mesh(
        mesh.devices.reshape(mesh.shape["pipe"], dp_size // 4, 2, 2),
        ("pipe",) + GROUP,
    )
    placed = (
        P(None, GROUP, None),
        P(None, GROUP, None),
        P("pipe", None),
        P("pipe", GROUP, None, None),
        P("pipe", None),
        P(None, GROUP),
    )
    return jax.shard_map(
        on_device,
        mesh=split,
        in_specs=placed,
        out_specs=(
            P("pipe", None, GROUP, None),
            P("pipe", None, GROUP, None),
            P("pipe", GROUP, None, None),
        ),
        check_vma=False,
    )
```

```python
import jax
import jax.numpy as jnp
from jax import lax
from jax.sharding import Mesh
from jax.sharding import PartitionSpec as P

TILE = 128
KEEP = 8
GROUP = ("dq", "zl", "core")


epsilon = 1e-05


def normalize(section_input, section_gain):
    values = section_input.astype(jnp.float32)
    inv_rms = lax.rsqrt(jnp.mean(values * values, axis=-1, keepdims=True) + epsilon)
    unit_rows = values * inv_rms
    return (values, inv_rms, unit_rows, (unit_rows * section_gain).astype(jnp.bfloat16))


def store_slot(buffer_all, new_value, micro_slot, is_live):
    old_value = lax.dynamic_index_in_dim(buffer_all, micro_slot, 0, keepdims=False)
    chosen = jnp.where(is_live, new_value, old_value)
    return lax.dynamic_update_index_in_dim(buffer_all, chosen, micro_slot, 0)


def reduce_tiles(hidden_rows, delta_rows, column_table):
    core = lax.axis_index("core")
    half = column_table.shape[1] // 2

    def tile_sums(columns):
        picked = jnp.take(delta_rows, columns, axis=1)
        return jnp.einsum("trk,trjn->rjkn", hidden_rows, picked, preferred_element_type=jnp.float32)

    send = tile_sums(lax.dynamic_slice_in_dim(column_table, (1 - core) * half, half, 1))
    got = lax.ppermute(send, "core", [(0, 1), (1, 0)])
    keep = tile_sums(lax.dynamic_slice_in_dim(column_table, core * half, half, 1))
    spread = lax.all_to_all(keep + got, ("dq", "zl"), 0, 0, tiled=True)
    return spread.sum(axis=0)


def gather_tiles(shard):
    chips = lax.axis_size("dq") * lax.axis_size("zl")
    sent = jnp.broadcast_to(shard[None], (chips,) + shard.shape)
    mine = lax.all_to_all(sent, ("dq", "zl"), 0, 0, tiled=True)
    other = lax.ppermute(mine, "core", [(0, 1), (1, 0)])
    return jnp.stack([mine, other], 1).reshape((-1,) + shard.shape[1:])


def on_device(acts_in, cotangent, norm_gains, weights, tile_columns, lengths):
    micro_count, row_count, model_width = acts_in.shape
    within = jnp.arange(row_count, dtype=jnp.int32)
    valid_rows = (within[None, :] < lengths).astype(jnp.float32)
    merged = (1, micro_count * row_count, model_width)
    section_out, input_grad, weight_grad = run_pipeline(
        acts_in.reshape(merged),
        cotangent.reshape(merged),
        norm_gains,
        weights,
        tile_columns,
        valid_rows.reshape(merged[:2]),
    )
    return (
        section_out.reshape(acts_in.shape)[None],
        input_grad.reshape(acts_in.shape)[None],
        weight_grad[None],
    )


def run_pipeline(acts_in, cotangent, norm_gains, weights, tile_columns, valid_rows):
    micro_count, row_count, model_width = acts_in.shape
    section_count = lax.axis_size("pipe")
    section_here = lax.axis_index("pipe")
    blocks = model_width // TILE
    section_gain = norm_gains[0]
    column_list = tile_columns[0]
    column_table = column_list.reshape(blocks, KEEP)
    gathered = gather_tiles(weights[0])
    tile_grid = gathered.reshape(blocks, KEEP, TILE, TILE)
    core = lax.axis_index("core")
    local_order = (jnp.arange(KEEP, dtype=jnp.int32) + (KEEP // 2) * core) % KEEP
    local_table = jnp.take(column_table, local_order, axis=1)
    onehot = (local_table[:, :, None] == jnp.arange(blocks, dtype=jnp.int32)).astype(jnp.bfloat16)
    dense = (
        jnp.einsum("rjkn,rjc->rkcn", tile_grid, onehot, preferred_element_type=jnp.float32)
        .astype(jnp.bfloat16)
        .reshape(model_width, model_width)
    )
    received = jnp.zeros((row_count, model_width), jnp.bfloat16)
    section_out = jnp.zeros_like(acts_in)
    saved_inputs = jnp.zeros_like(acts_in)
    saved_hidden = jnp.zeros_like(acts_in)
    saved_pre = jnp.zeros(acts_in.shape, jnp.float32)

    def run_forward(section_input):
        values, inv_rms, unit_rows, hidden = normalize(section_input, section_gain)
        pre_act = jnp.dot(hidden, dense, preferred_element_type=jnp.float32)
        return ((values + jax.nn.silu(pre_act)).astype(jnp.bfloat16), pre_act, hidden)

    def skip_forward(section_input):
        return (
            section_input,
            jnp.zeros((row_count, model_width), jnp.float32),
            jnp.zeros((row_count, model_width), jnp.bfloat16),
        )

    for clock_tick in range(micro_count + section_count - 1):
        micro_index = clock_tick - section_here
        is_live = jnp.logical_and(micro_index >= 0, micro_index < micro_count)
        micro_slot = jnp.clip(micro_index, 0, micro_count - 1)
        first_input = lax.dynamic_index_in_dim(acts_in, micro_slot, 0, keepdims=False)
        section_input = jnp.where(section_here == 0, first_input, received)
        section_result, pre_act, hidden = lax.cond(
            is_live, run_forward, skip_forward, section_input
        )
        section_out = store_slot(section_out, section_result, micro_slot, is_live)
        saved_inputs = store_slot(saved_inputs, section_input, micro_slot, is_live)
        saved_hidden = store_slot(saved_hidden, hidden, micro_slot, is_live)
        saved_pre = store_slot(saved_pre, pre_act, micro_slot, is_live)
        pairs = [
            (source, source + 1)
            for source in range(section_count - 1)
            if 0 <= clock_tick - source < micro_count
        ]
        if pairs:
            received = lax.ppermute(section_result, "pipe", pairs)

    def run_backward(section_input, grad_input, pre_act):
        values, inv_rms, unit_rows, hidden = normalize(section_input, section_gain)
        sigmoid_part = jax.nn.sigmoid(pre_act)
        grad_float = grad_input.astype(jnp.float32)
        pre_delta = (grad_float * sigmoid_part * (1.0 + pre_act * (1.0 - sigmoid_part))).astype(
            jnp.bfloat16
        )
        hidden_delta = lax.dot_general(
            pre_delta, dense, (((1,), (1,)), ((), ())), preferred_element_type=jnp.float32
        )
        gained = hidden_delta * section_gain
        input_delta = grad_float + inv_rms * (
            gained - unit_rows * jnp.mean(gained * unit_rows, axis=-1, keepdims=True)
        )
        return (input_delta.astype(jnp.bfloat16), pre_delta)

    def skip_backward(section_input, grad_input, pre_act):
        return (grad_input, jnp.zeros_like(grad_input))

    received = jnp.zeros((row_count, model_width), jnp.bfloat16)
    input_grad = jnp.zeros_like(acts_in)
    saved_delta = jnp.zeros_like(acts_in)
    for clock_tick in range(micro_count + section_count - 1):
        micro_index = clock_tick - (section_count - 1 - section_here)
        is_live = jnp.logical_and(micro_index >= 0, micro_index < micro_count)
        micro_slot = jnp.clip(micro_index, 0, micro_count - 1)
        last_cot = lax.dynamic_index_in_dim(cotangent, micro_slot, 0, keepdims=False).astype(
            jnp.float32
        )
        last_mask = lax.dynamic_index_in_dim(valid_rows, micro_slot, 0, keepdims=False)
        last_grad = (last_cot * last_mask[:, None]).astype(jnp.bfloat16)
        grad_input = jnp.where(section_here == section_count - 1, last_grad, received)
        section_input = lax.dynamic_index_in_dim(saved_inputs, micro_slot, 0, keepdims=False)
        pre_act = lax.dynamic_index_in_dim(saved_pre, micro_slot, 0, keepdims=False)
        input_delta, pre_delta = lax.cond(
            is_live, run_backward, skip_backward, section_input, grad_input, pre_act
        )
        input_grad = store_slot(input_grad, input_delta, micro_slot, is_live)
        saved_delta = store_slot(saved_delta, pre_delta, micro_slot, is_live)
        pairs = [
            (source, source - 1)
            for source in range(1, section_count)
            if 0 <= clock_tick - (section_count - 1 - source) < micro_count
        ]
        if pairs:
            received = lax.ppermute(input_delta, "pipe", pairs)
    all_rows = micro_count * row_count
    weight_grad = reduce_tiles(
        saved_hidden.reshape(all_rows, blocks, TILE),
        saved_delta.reshape(all_rows, blocks, TILE),
        column_table,
    )
    return (section_out, input_grad, weight_grad)


def solution(mesh):
    dp_size = mesh.shape["dp"]
    split = Mesh(
        mesh.devices.reshape(mesh.shape["pipe"], dp_size // 4, 2, 2),
        ("pipe",) + GROUP,
    )
    placed = (
        P(None, GROUP, None),
        P(None, GROUP, None),
        P("pipe", None),
        P("pipe", GROUP, None, None),
        P("pipe", None),
        P(None, GROUP),
    )
    return jax.shard_map(
        on_device,
        mesh=split,
        in_specs=placed,
        out_specs=(
            P("pipe", None, GROUP, None),
            P("pipe", None, GROUP, None),
            P("pipe", GROUP, None, None),
        ),
        check_vma=False,
    )
```

```python
import jax
import jax.numpy as jnp
from jax import lax
from jax.sharding import Mesh
from jax.sharding import PartitionSpec as P

TILE = 128
KEEP = 8
GROUP = ("dq", "zl", "core")


epsilon = 1e-05


def normalize(section_input, section_gain):
    values = section_input.astype(jnp.float32)
    inv_rms = lax.rsqrt(jnp.mean(values * values, axis=-1, keepdims=True) + epsilon)
    unit_rows = values * inv_rms
    return (values, inv_rms, unit_rows, (unit_rows * section_gain).astype(jnp.bfloat16))


def store_slot(buffer_all, new_value, micro_slot, is_live):
    old_value = lax.dynamic_index_in_dim(buffer_all, micro_slot, 0, keepdims=False)
    chosen = jnp.where(is_live, new_value, old_value)
    return lax.dynamic_update_index_in_dim(buffer_all, chosen, micro_slot, 0)


def reduce_tiles(hidden_rows, delta_rows, column_table):
    core = lax.axis_index("core")
    half = column_table.shape[1] // 2

    def tile_sums(columns):
        picked = jnp.take(delta_rows, columns, axis=1)
        return jnp.einsum("trk,trjn->rjkn", hidden_rows, picked, preferred_element_type=jnp.float32)

    send = tile_sums(lax.dynamic_slice_in_dim(column_table, (1 - core) * half, half, 1))
    got = lax.ppermute(send, "core", [(0, 1), (1, 0)])
    keep = tile_sums(lax.dynamic_slice_in_dim(column_table, core * half, half, 1))
    spread = lax.all_to_all(keep + got, ("dq", "zl"), 0, 0, tiled=True)
    return spread.sum(axis=0)


def gather_tiles(shard):
    chips = lax.axis_size("dq") * lax.axis_size("zl")
    sent = jnp.broadcast_to(shard[None], (chips,) + shard.shape)
    mine = lax.all_to_all(sent, ("dq", "zl"), 0, 0, tiled=True)
    other = lax.ppermute(mine, "core", [(0, 1), (1, 0)])
    return jnp.stack([mine, other], 1).reshape((-1,) + shard.shape[1:])


def on_device(acts_in, cotangent, norm_gains, weights, tile_columns, lengths):
    micro_count, row_count, model_width = acts_in.shape
    within = jnp.arange(row_count, dtype=jnp.int32)
    valid_rows = (within[None, :] < lengths).astype(jnp.float32)
    merged = (1, micro_count * row_count, model_width)
    section_out, input_grad, weight_grad = run_pipeline(
        acts_in.reshape(merged),
        cotangent.reshape(merged),
        norm_gains,
        weights,
        tile_columns,
        valid_rows.reshape(merged[:2]),
    )
    return (
        section_out.reshape(acts_in.shape)[None],
        input_grad.reshape(acts_in.shape)[None],
        weight_grad[None],
    )


def run_pipeline(acts_in, cotangent, norm_gains, weights, tile_columns, valid_rows):
    micro_count, row_count, model_width = acts_in.shape
    section_count = lax.axis_size("pipe")
    section_here = lax.axis_index("pipe")
    blocks = model_width // TILE
    section_gain = norm_gains[0]
    column_list = tile_columns[0]
    column_table = column_list.reshape(blocks, KEEP)
    gathered = gather_tiles(weights[0])
    tile_grid = gathered.reshape(blocks, KEEP, TILE, TILE)
    core = lax.axis_index("core")
    local_order = (jnp.arange(KEEP, dtype=jnp.int32) + (KEEP // 2) * core) % KEEP
    local_table = jnp.take(column_table, local_order, axis=1)
    onehot = (local_table[:, :, None] == jnp.arange(blocks, dtype=jnp.int32)).astype(jnp.bfloat16)
    dense = (
        jnp.einsum("rjkn,rjc->rkcn", tile_grid, onehot, preferred_element_type=jnp.float32)
        .astype(jnp.bfloat16)
        .reshape(model_width, model_width)
    )
    received = jnp.zeros((row_count, model_width), jnp.bfloat16)
    section_out = jnp.zeros_like(acts_in)
    saved_inputs = jnp.zeros_like(acts_in)
    saved_hidden = jnp.zeros_like(acts_in)
    saved_pre = jnp.zeros(acts_in.shape, jnp.float32)

    def run_forward(section_input):
        values, inv_rms, unit_rows, hidden = normalize(section_input, section_gain)
        pre_act = jnp.dot(hidden, dense, preferred_element_type=jnp.float32)
        return ((values + jax.nn.silu(pre_act)).astype(jnp.bfloat16), pre_act, hidden)

    def first_forward(section_input):
        values, inv_rms, unit_rows, hidden = normalize(section_input, section_gain)
        tile_parts = jnp.einsum(
            "trk,rjkn->trjn",
            hidden.reshape(row_count, blocks, TILE),
            tile_grid,
            preferred_element_type=jnp.float32,
        )
        pre_act = jnp.einsum(
            "trjn,rjc->tcn",
            tile_parts,
            onehot.astype(jnp.float32),
            precision=lax.Precision.HIGHEST,
            preferred_element_type=jnp.float32,
        ).reshape(row_count, model_width)
        return ((values + jax.nn.silu(pre_act)).astype(jnp.bfloat16), pre_act, hidden)

    def skip_forward(section_input):
        return (
            section_input,
            jnp.zeros((row_count, model_width), jnp.float32),
            jnp.zeros((row_count, model_width), jnp.bfloat16),
        )

    for clock_tick in range(micro_count + section_count - 1):
        micro_index = clock_tick - section_here
        is_live = jnp.logical_and(micro_index >= 0, micro_index < micro_count)
        micro_slot = jnp.clip(micro_index, 0, micro_count - 1)
        first_input = lax.dynamic_index_in_dim(acts_in, micro_slot, 0, keepdims=False)
        section_input = jnp.where(section_here == 0, first_input, received)
        section_result, pre_act, hidden = lax.cond(
            is_live, first_forward if clock_tick == 0 else run_forward, skip_forward, section_input
        )
        section_out = store_slot(section_out, section_result, micro_slot, is_live)
        saved_inputs = store_slot(saved_inputs, section_input, micro_slot, is_live)
        saved_hidden = store_slot(saved_hidden, hidden, micro_slot, is_live)
        saved_pre = store_slot(saved_pre, pre_act, micro_slot, is_live)
        pairs = [
            (source, source + 1)
            for source in range(section_count - 1)
            if 0 <= clock_tick - source < micro_count
        ]
        if pairs:
            received = lax.ppermute(section_result, "pipe", pairs)

    def run_backward(section_input, grad_input, pre_act):
        values, inv_rms, unit_rows, hidden = normalize(section_input, section_gain)
        sigmoid_part = jax.nn.sigmoid(pre_act)
        grad_float = grad_input.astype(jnp.float32)
        pre_delta = (grad_float * sigmoid_part * (1.0 + pre_act * (1.0 - sigmoid_part))).astype(
            jnp.bfloat16
        )
        hidden_delta = lax.dot_general(
            pre_delta, dense, (((1,), (1,)), ((), ())), preferred_element_type=jnp.float32
        )
        gained = hidden_delta * section_gain
        input_delta = grad_float + inv_rms * (
            gained - unit_rows * jnp.mean(gained * unit_rows, axis=-1, keepdims=True)
        )
        return (input_delta.astype(jnp.bfloat16), pre_delta)

    def skip_backward(section_input, grad_input, pre_act):
        return (grad_input, jnp.zeros_like(grad_input))

    received = jnp.zeros((row_count, model_width), jnp.bfloat16)
    input_grad = jnp.zeros_like(acts_in)
    saved_delta = jnp.zeros_like(acts_in)
    for clock_tick in range(micro_count + section_count - 1):
        micro_index = clock_tick - (section_count - 1 - section_here)
        is_live = jnp.logical_and(micro_index >= 0, micro_index < micro_count)
        micro_slot = jnp.clip(micro_index, 0, micro_count - 1)
        last_cot = lax.dynamic_index_in_dim(cotangent, micro_slot, 0, keepdims=False).astype(
            jnp.float32
        )
        last_mask = lax.dynamic_index_in_dim(valid_rows, micro_slot, 0, keepdims=False)
        last_grad = (last_cot * last_mask[:, None]).astype(jnp.bfloat16)
        grad_input = jnp.where(section_here == section_count - 1, last_grad, received)
        section_input = lax.dynamic_index_in_dim(saved_inputs, micro_slot, 0, keepdims=False)
        pre_act = lax.dynamic_index_in_dim(saved_pre, micro_slot, 0, keepdims=False)
        input_delta, pre_delta = lax.cond(
            is_live, run_backward, skip_backward, section_input, grad_input, pre_act
        )
        input_grad = store_slot(input_grad, input_delta, micro_slot, is_live)
        saved_delta = store_slot(saved_delta, pre_delta, micro_slot, is_live)
        pairs = [
            (source, source - 1)
            for source in range(1, section_count)
            if 0 <= clock_tick - (section_count - 1 - source) < micro_count
        ]
        if pairs:
            received = lax.ppermute(input_delta, "pipe", pairs)
    all_rows = micro_count * row_count
    weight_grad = reduce_tiles(
        saved_hidden.reshape(all_rows, blocks, TILE),
        saved_delta.reshape(all_rows, blocks, TILE),
        column_table,
    )
    return (section_out, input_grad, weight_grad)


def solution(mesh):
    dp_size = mesh.shape["dp"]
    split = Mesh(
        mesh.devices.reshape(mesh.shape["pipe"], dp_size // 4, 2, 2),
        ("pipe",) + GROUP,
    )
    placed = (
        P(None, GROUP, None),
        P(None, GROUP, None),
        P("pipe", None),
        P("pipe", GROUP, None, None),
        P("pipe", None),
        P(None, GROUP),
    )
    return jax.shard_map(
        on_device,
        mesh=split,
        in_specs=placed,
        out_specs=(
            P("pipe", None, GROUP, None),
            P("pipe", None, GROUP, None),
            P("pipe", GROUP, None, None),
        ),
        check_vma=False,
    )
```

```python
import jax
import jax.numpy as jnp
from jax import lax
from jax.sharding import Mesh
from jax.sharding import PartitionSpec as P

TILE = 128
KEEP = 8
GROUP = ("dq", "zl", "core")


epsilon = 1e-05


def normalize(section_input, section_gain):
    values = section_input.astype(jnp.float32)
    inv_rms = lax.rsqrt(jnp.mean(values * values, axis=-1, keepdims=True) + epsilon)
    unit_rows = values * inv_rms
    return (values, inv_rms, unit_rows, (unit_rows * section_gain).astype(jnp.bfloat16))


def store_slot(buffer_all, new_value, micro_slot, is_live):
    old_value = lax.dynamic_index_in_dim(buffer_all, micro_slot, 0, keepdims=False)
    chosen = jnp.where(is_live, new_value, old_value)
    return lax.dynamic_update_index_in_dim(buffer_all, chosen, micro_slot, 0)


def reduce_tiles(hidden_rows, delta_rows, column_table):
    core = lax.axis_index("core")
    half = column_table.shape[1] // 2

    def tile_sums(columns):
        picked = jnp.take(delta_rows, columns, axis=1)
        return jnp.einsum("trk,trjn->rjkn", hidden_rows, picked, preferred_element_type=jnp.float32)

    send = tile_sums(lax.dynamic_slice_in_dim(column_table, (1 - core) * half, half, 1))
    got = lax.ppermute(send, "core", [(0, 1), (1, 0)])
    keep = tile_sums(lax.dynamic_slice_in_dim(column_table, core * half, half, 1))
    spread = lax.all_to_all(keep + got, ("dq", "zl"), 0, 0, tiled=True)
    return spread.sum(axis=0)


def gather_tiles(shard):
    chips = lax.axis_size("dq") * lax.axis_size("zl")
    sent = jnp.broadcast_to(shard[None], (chips,) + shard.shape)
    mine = lax.all_to_all(sent, ("dq", "zl"), 0, 0, tiled=True)
    other = lax.ppermute(mine, "core", [(0, 1), (1, 0)])
    return jnp.stack([mine, other], 1).reshape((-1,) + shard.shape[1:])


def on_device(acts_in, cotangent, norm_gains, weights, tile_columns, lengths):
    micro_count, row_count, model_width = acts_in.shape
    within = jnp.arange(row_count, dtype=jnp.int32)
    valid_rows = (within[None, :] < lengths).astype(jnp.float32)
    merged = (1, micro_count * row_count, model_width)
    section_out, input_grad, weight_grad = run_pipeline(
        acts_in.reshape(merged),
        cotangent.reshape(merged),
        norm_gains,
        weights,
        tile_columns,
        valid_rows.reshape(merged[:2]),
    )
    return (
        section_out.reshape(acts_in.shape)[None],
        input_grad.reshape(acts_in.shape)[None],
        weight_grad[None],
    )


def run_pipeline(acts_in, cotangent, norm_gains, weights, tile_columns, valid_rows):
    micro_count, row_count, model_width = acts_in.shape
    section_count = lax.axis_size("pipe")
    section_here = lax.axis_index("pipe")
    blocks = model_width // TILE
    section_gain = norm_gains[0]
    column_list = tile_columns[0]
    column_table = column_list.reshape(blocks, KEEP)
    gathered = gather_tiles(weights[0])
    tile_grid = gathered.reshape(blocks, KEEP, TILE, TILE)
    core = lax.axis_index("core")
    local_order = (jnp.arange(KEEP, dtype=jnp.int32) + (KEEP // 2) * core) % KEEP
    local_table = jnp.take(column_table, local_order, axis=1)
    onehot = (local_table[:, :, None] == jnp.arange(blocks, dtype=jnp.int32)).astype(jnp.bfloat16)
    dense = (
        jnp.einsum("rjkn,rjc->rkcn", tile_grid, onehot, preferred_element_type=jnp.float32)
        .astype(jnp.bfloat16)
        .reshape(model_width, model_width)
    )
    received = jnp.zeros((row_count, model_width), jnp.bfloat16)
    section_out = jnp.zeros_like(acts_in)
    saved_inputs = jnp.zeros_like(acts_in)
    saved_hidden = jnp.zeros_like(acts_in)
    saved_pre = jnp.zeros(acts_in.shape, jnp.float32)

    def run_forward(section_input):
        values, inv_rms, unit_rows, hidden = normalize(section_input, section_gain)
        pre_act = jnp.dot(hidden, dense, preferred_element_type=jnp.float32)
        return ((values + jax.nn.silu(pre_act)).astype(jnp.bfloat16), pre_act, hidden)

    def first_forward(section_input):
        values, inv_rms, unit_rows, hidden = normalize(section_input, section_gain)
        tile_parts = jnp.einsum(
            "trk,rjkn->trjn",
            hidden.reshape(row_count, blocks, TILE),
            tile_grid,
            preferred_element_type=jnp.float32,
        )
        pre_act = jnp.einsum(
            "trjn,rjc->tcn",
            tile_parts,
            onehot.astype(jnp.float32),
            precision=lax.Precision.HIGH,
            preferred_element_type=jnp.float32,
        ).reshape(row_count, model_width)
        return ((values + jax.nn.silu(pre_act)).astype(jnp.bfloat16), pre_act, hidden)

    def skip_forward(section_input):
        return (
            section_input,
            jnp.zeros((row_count, model_width), jnp.float32),
            jnp.zeros((row_count, model_width), jnp.bfloat16),
        )

    for clock_tick in range(micro_count + section_count - 1):
        micro_index = clock_tick - section_here
        is_live = jnp.logical_and(micro_index >= 0, micro_index < micro_count)
        micro_slot = jnp.clip(micro_index, 0, micro_count - 1)
        first_input = lax.dynamic_index_in_dim(acts_in, micro_slot, 0, keepdims=False)
        section_input = jnp.where(section_here == 0, first_input, received)
        section_result, pre_act, hidden = lax.cond(
            is_live, first_forward if clock_tick == 0 else run_forward, skip_forward, section_input
        )
        section_out = store_slot(section_out, section_result, micro_slot, is_live)
        saved_inputs = store_slot(saved_inputs, section_input, micro_slot, is_live)
        saved_hidden = store_slot(saved_hidden, hidden, micro_slot, is_live)
        saved_pre = store_slot(saved_pre, pre_act, micro_slot, is_live)
        pairs = [
            (source, source + 1)
            for source in range(section_count - 1)
            if 0 <= clock_tick - source < micro_count
        ]
        if pairs:
            received = lax.ppermute(section_result, "pipe", pairs)

    def run_backward(section_input, grad_input, pre_act):
        values, inv_rms, unit_rows, hidden = normalize(section_input, section_gain)
        sigmoid_part = jax.nn.sigmoid(pre_act)
        grad_float = grad_input.astype(jnp.float32)
        pre_delta = (grad_float * sigmoid_part * (1.0 + pre_act * (1.0 - sigmoid_part))).astype(
            jnp.bfloat16
        )
        hidden_delta = lax.dot_general(
            pre_delta, dense, (((1,), (1,)), ((), ())), preferred_element_type=jnp.float32
        )
        gained = hidden_delta * section_gain
        input_delta = grad_float + inv_rms * (
            gained - unit_rows * jnp.mean(gained * unit_rows, axis=-1, keepdims=True)
        )
        return (input_delta.astype(jnp.bfloat16), pre_delta)

    def skip_backward(section_input, grad_input, pre_act):
        return (grad_input, jnp.zeros_like(grad_input))

    received = jnp.zeros((row_count, model_width), jnp.bfloat16)
    input_grad = jnp.zeros_like(acts_in)
    saved_delta = jnp.zeros_like(acts_in)
    for clock_tick in range(micro_count + section_count - 1):
        micro_index = clock_tick - (section_count - 1 - section_here)
        is_live = jnp.logical_and(micro_index >= 0, micro_index < micro_count)
        micro_slot = jnp.clip(micro_index, 0, micro_count - 1)
        last_cot = lax.dynamic_index_in_dim(cotangent, micro_slot, 0, keepdims=False).astype(
            jnp.float32
        )
        last_mask = lax.dynamic_index_in_dim(valid_rows, micro_slot, 0, keepdims=False)
        last_grad = (last_cot * last_mask[:, None]).astype(jnp.bfloat16)
        grad_input = jnp.where(section_here == section_count - 1, last_grad, received)
        section_input = lax.dynamic_index_in_dim(saved_inputs, micro_slot, 0, keepdims=False)
        pre_act = lax.dynamic_index_in_dim(saved_pre, micro_slot, 0, keepdims=False)
        input_delta, pre_delta = lax.cond(
            is_live, run_backward, skip_backward, section_input, grad_input, pre_act
        )
        input_grad = store_slot(input_grad, input_delta, micro_slot, is_live)
        saved_delta = store_slot(saved_delta, pre_delta, micro_slot, is_live)
        pairs = [
            (source, source - 1)
            for source in range(1, section_count)
            if 0 <= clock_tick - (section_count - 1 - source) < micro_count
        ]
        if pairs:
            received = lax.ppermute(input_delta, "pipe", pairs)
    all_rows = micro_count * row_count
    weight_grad = reduce_tiles(
        saved_hidden.reshape(all_rows, blocks, TILE),
        saved_delta.reshape(all_rows, blocks, TILE),
        column_table,
    )
    return (section_out, input_grad, weight_grad)


def solution(mesh):
    dp_size = mesh.shape["dp"]
    split = Mesh(
        mesh.devices.reshape(mesh.shape["pipe"], dp_size // 4, 2, 2),
        ("pipe",) + GROUP,
    )
    placed = (
        P(None, GROUP, None),
        P(None, GROUP, None),
        P("pipe", None),
        P("pipe", GROUP, None, None),
        P("pipe", None),
        P(None, GROUP),
    )
    return jax.shard_map(
        on_device,
        mesh=split,
        in_specs=placed,
        out_specs=(
            P("pipe", None, GROUP, None),
            P("pipe", None, GROUP, None),
            P("pipe", GROUP, None, None),
        ),
        check_vma=False,
    )
```

```python
import jax
import jax.numpy as jnp
from jax import lax
from jax.sharding import Mesh
from jax.sharding import PartitionSpec as P

TILE = 128
KEEP = 8
GROUP = ("dq", "zl", "core")


epsilon = 1e-05


def normalize(section_input, section_gain):
    values = section_input.astype(jnp.float32)
    inv_rms = lax.rsqrt(jnp.mean(values * values, axis=-1, keepdims=True) + epsilon)
    unit_rows = values * inv_rms
    return (values, inv_rms, unit_rows, (unit_rows * section_gain).astype(jnp.bfloat16))


def store_slot(buffer_all, new_value, micro_slot, is_live):
    old_value = lax.dynamic_index_in_dim(buffer_all, micro_slot, 0, keepdims=False)
    chosen = jnp.where(is_live, new_value, old_value)
    return lax.dynamic_update_index_in_dim(buffer_all, chosen, micro_slot, 0)


def reduce_tiles(hidden_rows, delta_rows, column_table):
    core = lax.axis_index("core")
    half = column_table.shape[1] // 2

    def tile_sums(columns):
        picked = jnp.take(delta_rows, columns, axis=1)
        return jnp.einsum("trk,trjn->rjkn", hidden_rows, picked, preferred_element_type=jnp.float32)

    send = tile_sums(lax.dynamic_slice_in_dim(column_table, (1 - core) * half, half, 1))
    got = lax.ppermute(send, "core", [(0, 1), (1, 0)])
    keep = tile_sums(lax.dynamic_slice_in_dim(column_table, core * half, half, 1))
    spread = lax.all_to_all(keep + got, ("dq", "zl"), 0, 0, tiled=True)
    return spread.sum(axis=0)


def gather_tiles(shard):
    chips = lax.axis_size("dq") * lax.axis_size("zl")
    sent = jnp.broadcast_to(shard[None], (chips,) + shard.shape)
    mine = lax.all_to_all(sent, ("dq", "zl"), 0, 0, tiled=True)
    other = lax.ppermute(mine, "core", [(0, 1), (1, 0)])
    return mine, other


def on_device(acts_in, cotangent, norm_gains, weights, tile_columns, lengths):
    micro_count, row_count, model_width = acts_in.shape
    within = jnp.arange(row_count, dtype=jnp.int32)
    valid_rows = (within[None, :] < lengths).astype(jnp.float32)
    merged = (1, micro_count * row_count, model_width)
    section_out, input_grad, weight_grad = run_pipeline(
        acts_in.reshape(merged),
        cotangent.reshape(merged),
        norm_gains,
        weights,
        tile_columns,
        valid_rows.reshape(merged[:2]),
    )
    return (
        section_out.reshape(acts_in.shape)[None],
        input_grad.reshape(acts_in.shape)[None],
        weight_grad[None],
    )


def run_pipeline(acts_in, cotangent, norm_gains, weights, tile_columns, valid_rows):
    micro_count, row_count, model_width = acts_in.shape
    section_count = lax.axis_size("pipe")
    section_here = lax.axis_index("pipe")
    blocks = model_width // TILE
    section_gain = norm_gains[0]
    column_list = tile_columns[0]
    column_table = column_list.reshape(blocks, KEEP)
    mine, other = gather_tiles(weights[0])
    tile_grid = jnp.stack([mine, other], 1).reshape(blocks, KEEP, TILE, TILE)
    core = lax.axis_index("core")
    local_order = (jnp.arange(KEEP, dtype=jnp.int32) + (KEEP // 2) * core) % KEEP
    local_table = jnp.take(column_table, local_order, axis=1)
    onehot = (local_table[:, :, None] == jnp.arange(blocks, dtype=jnp.int32)).astype(jnp.bfloat16)
    dense = (
        jnp.einsum("rjkn,rjc->rkcn", tile_grid, onehot, preferred_element_type=jnp.float32)
        .astype(jnp.bfloat16)
        .reshape(model_width, model_width)
    )
    received = jnp.zeros((row_count, model_width), jnp.bfloat16)
    section_out = jnp.zeros_like(acts_in)
    saved_inputs = jnp.zeros_like(acts_in)
    saved_hidden = jnp.zeros_like(acts_in)
    saved_pre = jnp.zeros(acts_in.shape, jnp.float32)

    def run_forward(section_input):
        values, inv_rms, unit_rows, hidden = normalize(section_input, section_gain)
        pre_act = jnp.dot(hidden, dense, preferred_element_type=jnp.float32)
        return ((values + jax.nn.silu(pre_act)).astype(jnp.bfloat16), pre_act, hidden)

    def first_forward(section_input):
        values, inv_rms, unit_rows, hidden = normalize(section_input, section_gain)
        half = KEEP // 2
        pre_act = 0.0
        for tiles, picks in ((mine, onehot[:, :half]), (other, onehot[:, half:])):
            tile_parts = jnp.einsum(
                "trk,rjkn->trjn",
                hidden.reshape(row_count, blocks, TILE),
                tiles,
                preferred_element_type=jnp.float32,
            )
            pre_act = pre_act + jnp.einsum(
                "trjn,rjc->tcn",
                tile_parts,
                picks.astype(jnp.float32),
                precision=lax.Precision.HIGHEST,
                preferred_element_type=jnp.float32,
            )
        pre_act = pre_act.reshape(row_count, model_width)
        return ((values + jax.nn.silu(pre_act)).astype(jnp.bfloat16), pre_act, hidden)

    def skip_forward(section_input):
        return (
            section_input,
            jnp.zeros((row_count, model_width), jnp.float32),
            jnp.zeros((row_count, model_width), jnp.bfloat16),
        )

    for clock_tick in range(micro_count + section_count - 1):
        micro_index = clock_tick - section_here
        is_live = jnp.logical_and(micro_index >= 0, micro_index < micro_count)
        micro_slot = jnp.clip(micro_index, 0, micro_count - 1)
        first_input = lax.dynamic_index_in_dim(acts_in, micro_slot, 0, keepdims=False)
        section_input = jnp.where(section_here == 0, first_input, received)
        section_result, pre_act, hidden = lax.cond(
            is_live, first_forward if clock_tick == 0 else run_forward, skip_forward, section_input
        )
        section_out = store_slot(section_out, section_result, micro_slot, is_live)
        saved_inputs = store_slot(saved_inputs, section_input, micro_slot, is_live)
        saved_hidden = store_slot(saved_hidden, hidden, micro_slot, is_live)
        saved_pre = store_slot(saved_pre, pre_act, micro_slot, is_live)
        pairs = [
            (source, source + 1)
            for source in range(section_count - 1)
            if 0 <= clock_tick - source < micro_count
        ]
        if pairs:
            received = lax.ppermute(section_result, "pipe", pairs)

    def run_backward(section_input, grad_input, pre_act):
        values, inv_rms, unit_rows, hidden = normalize(section_input, section_gain)
        sigmoid_part = jax.nn.sigmoid(pre_act)
        grad_float = grad_input.astype(jnp.float32)
        pre_delta = (grad_float * sigmoid_part * (1.0 + pre_act * (1.0 - sigmoid_part))).astype(
            jnp.bfloat16
        )
        hidden_delta = lax.dot_general(
            pre_delta, dense, (((1,), (1,)), ((), ())), preferred_element_type=jnp.float32
        )
        gained = hidden_delta * section_gain
        input_delta = grad_float + inv_rms * (
            gained - unit_rows * jnp.mean(gained * unit_rows, axis=-1, keepdims=True)
        )
        return (input_delta.astype(jnp.bfloat16), pre_delta)

    def skip_backward(section_input, grad_input, pre_act):
        return (grad_input, jnp.zeros_like(grad_input))

    received = jnp.zeros((row_count, model_width), jnp.bfloat16)
    input_grad = jnp.zeros_like(acts_in)
    saved_delta = jnp.zeros_like(acts_in)
    for clock_tick in range(micro_count + section_count - 1):
        micro_index = clock_tick - (section_count - 1 - section_here)
        is_live = jnp.logical_and(micro_index >= 0, micro_index < micro_count)
        micro_slot = jnp.clip(micro_index, 0, micro_count - 1)
        last_cot = lax.dynamic_index_in_dim(cotangent, micro_slot, 0, keepdims=False).astype(
            jnp.float32
        )
        last_mask = lax.dynamic_index_in_dim(valid_rows, micro_slot, 0, keepdims=False)
        last_grad = (last_cot * last_mask[:, None]).astype(jnp.bfloat16)
        grad_input = jnp.where(section_here == section_count - 1, last_grad, received)
        section_input = lax.dynamic_index_in_dim(saved_inputs, micro_slot, 0, keepdims=False)
        pre_act = lax.dynamic_index_in_dim(saved_pre, micro_slot, 0, keepdims=False)
        input_delta, pre_delta = lax.cond(
            is_live, run_backward, skip_backward, section_input, grad_input, pre_act
        )
        input_grad = store_slot(input_grad, input_delta, micro_slot, is_live)
        saved_delta = store_slot(saved_delta, pre_delta, micro_slot, is_live)
        pairs = [
            (source, source - 1)
            for source in range(1, section_count)
            if 0 <= clock_tick - (section_count - 1 - source) < micro_count
        ]
        if pairs:
            received = lax.ppermute(input_delta, "pipe", pairs)
    all_rows = micro_count * row_count
    weight_grad = reduce_tiles(
        saved_hidden.reshape(all_rows, blocks, TILE),
        saved_delta.reshape(all_rows, blocks, TILE),
        column_table,
    )
    return (section_out, input_grad, weight_grad)


def solution(mesh):
    dp_size = mesh.shape["dp"]
    split = Mesh(
        mesh.devices.reshape(mesh.shape["pipe"], dp_size // 4, 2, 2),
        ("pipe",) + GROUP,
    )
    placed = (
        P(None, GROUP, None),
        P(None, GROUP, None),
        P("pipe", None),
        P("pipe", GROUP, None, None),
        P("pipe", None),
        P(None, GROUP),
    )
    return jax.shard_map(
        on_device,
        mesh=split,
        in_specs=placed,
        out_specs=(
            P("pipe", None, GROUP, None),
            P("pipe", None, GROUP, None),
            P("pipe", GROUP, None, None),
        ),
        check_vma=False,
    )
```
